128 devices in a mesh: ctx: 16 (over x, y_lo, core), tp: 8 (over y_hi, z).
Axes of the slice: x: 4, y: 4 (y_hi: 2, y_lo: 2; y = y_hi * 2 + y_lo), z: 4, core: 2. Of those that a mesh axis runs over, the one named last changes fastest.
Arguments:
- ctx_queries: bfloat16 [16384, 8192], P('ctx', 'tp'), may hold values from -70 to 70
- context_key_rows: bfloat16 [16384, 1024], P('ctx', 'tp'), may hold values from -4 to 4
- context_value_rows: bfloat16 [16384, 1024], P('ctx', 'tp'), may hold values from -6 to 6
- resp_queries: bfloat16 [512, 8192], P('ctx', 'tp'), may hold values from -70 to 70
- resp_keys: bfloat16 [512, 1024], P('ctx', 'tp'), may hold values from -4 to 4
- response_value_rows: bfloat16 [512, 1024], P('ctx', 'tp'), may hold values from -6 to 6
- split_index: int32 [1], replicated, may hold values from 64 to 448
- out_weight: bfloat16 [8192, 8192], P('tp'), may hold values from -0.0625 to 0.0625
Outputs:
- ctx_out: float32 [16384, 8192], P('ctx', 'tp')
- resp_out: float32 [512, 8192], P('ctx', 'tp')
The draws below stay inside these ranges and needn't reach their ends.
All inputs are finite; a program needn't handle non-finite values.
Results may differ from the reference program's by a relative error of at most 0.005.
Values may be sent and summed in bfloat16 or wider, within the bound.
No kernel may reach another device: no remote copies, remote signals or barrier semaphores. Data moves between devices by JAX's collectives and lax.ppermute only.
A program may use at most 192 MiB of HBM per device.

```python
import jax
import jax.numpy as jnp
from jax import lax

D = 8192
QUERY_HEADS = 64
KEY_VALUE_HEADS = 8
HEAD_WIDTH = 128
CONTEXT_BLOCK = 1024
CONTEXT_TOKENS = 16384
RESPONSE_ROWS = 512


def context_keys(key):
    random_seed_key = jax.random.fold_in(key, 101)
    sampled_arrays = jax.random.truncated_normal(random_seed_key, -4.0, 4.0, (CONTEXT_TOKENS, KEY_VALUE_HEADS * HEAD_WIDTH), jnp.float32)
    return sampled_arrays


def response_keys(key):
    random_seed_key = jax.random.fold_in(key, 202)
    sampled_arrays = jax.random.truncated_normal(random_seed_key, -4.0, 4.0, (RESPONSE_ROWS, KEY_VALUE_HEADS * HEAD_WIDTH), jnp.float32)
    return sampled_arrays


def draw_context_key_rows(key, part):
    return context_keys(key).astype(jnp.bfloat16)


def draw_resp_keys(key, part):
    return response_keys(key).astype(jnp.bfloat16)


def draw_ctx_queries(key, part):
    random_seed_key = jax.random.fold_in(key, 303)
    sampled_arrays = 3.0 * jax.random.truncated_normal(random_seed_key, -4.0, 4.0, (CONTEXT_TOKENS, QUERY_HEADS * HEAD_WIDTH), jnp.float32)
    return sampled_arrays.astype(jnp.bfloat16)


def draw_resp_queries(key, part):
    random_seed_key = jax.random.fold_in(key, 404)
    sampled_arrays = 3.0 * jax.random.truncated_normal(random_seed_key, -4.0, 4.0, (RESPONSE_ROWS, QUERY_HEADS * HEAD_WIDTH), jnp.float32)
    return sampled_arrays.astype(jnp.bfloat16)


def steps_of(rng, dims, split, smallest, top_value):
    gain = 1.0
    for axis_at, parts in split:
        steps = jax.random.uniform(jax.random.fold_in(jax.random.fold_in(rng, 6), axis_at), (parts,), jnp.float32, smallest / len(split), top_value / len(split))
        gain = gain * jnp.repeat(jnp.exp(steps), dims[axis_at] // parts).reshape((-1,) + (1,) * (len(dims) - 1 - axis_at))
    return gain


def gaussian(stream_key, dims, spread, bound, cuts=(), kind=jnp.bfloat16):
    loudness = steps_of(stream_key, dims, cuts, -0.22, 0.18) if cuts else 1.0
    drawn = jax.random.normal(stream_key, dims, jnp.float32) * spread * loudness
    return jnp.minimum(jnp.maximum(drawn, -bound), bound).astype(kind)


def setup_inputs(seed: int = 0) -> dict:
    key_of = jax.random.split(jax.random.key(seed), 9)
    return {
        "ctx_queries": draw_ctx_queries(jax.random.fold_in(key_of[8], 71), 0),
        "context_key_rows": draw_context_key_rows(jax.random.fold_in(key_of[8], 71), 0),
        "context_value_rows": gaussian(key_of[2], (CONTEXT_TOKENS, KEY_VALUE_HEADS * HEAD_WIDTH), 1.0, 6.0, ((0, 16), (1, 8))),
        "resp_queries": draw_resp_queries(jax.random.fold_in(key_of[8], 71), 0),
        "resp_keys": draw_resp_keys(jax.random.fold_in(key_of[8], 71), 0),
        "response_value_rows": gaussian(key_of[5], (RESPONSE_ROWS, KEY_VALUE_HEADS * HEAD_WIDTH), 1.0, 6.0, ((0, 16), (1, 8))),
        "split_index": jax.random.randint(key_of[6], (1,), RESPONSE_ROWS // 8, 7 * RESPONSE_ROWS // 8 + 1).astype(jnp.int32),
        "out_weight": gaussian(key_of[7], (QUERY_HEADS * HEAD_WIDTH, D), (QUERY_HEADS * HEAD_WIDTH) ** -0.5, 0.0625, ((0, 8),)),
    }


NEGATIVE = -1.0e30


def partial_softmax(queries, key_rows, value_rows, visible, head_size):
    query_count = queries.shape[0]
    kv_heads = key_rows.shape[1] // head_size
    query_heads = queries.shape[1] // head_size
    group_size = query_heads // kv_heads
    score_scale = head_size ** -0.5
    stacked_queries = queries.reshape(query_count, query_heads, head_size).transpose(1, 0, 2)
    stacked_keys = key_rows.reshape(-1, kv_heads, head_size).transpose(1, 0, 2)
    stacked_values = value_rows.reshape(-1, kv_heads, head_size).transpose(1, 0, 2)

    def one_head(inputs):
        head_query, head_index = inputs
        head_keys = lax.dynamic_index_in_dim(stacked_keys, head_index // group_size, 0, keepdims=False)
        head_values = lax.dynamic_index_in_dim(stacked_values, head_index // group_size, 0, keepdims=False)
        scores = jnp.dot(head_query, head_keys.T, preferred_element_type=jnp.float32) * score_scale
        scores = jnp.where(visible, scores, NEGATIVE)
        row_max = jnp.max(scores, axis=1)
        weights = jnp.where(visible, jnp.exp(scores - row_max[:, None]), 0.0)
        row_sum = jnp.sum(weights, axis=1)
        numerator = jnp.dot(weights.astype(jnp.bfloat16), head_values, preferred_element_type=jnp.float32)
        return row_max, row_sum, numerator

    maxima, totals, numerator = lax.map(one_head, (stacked_queries, jnp.arange(query_heads, dtype=jnp.int32)))
    return maxima.T, totals.T, numerator.transpose(1, 0, 2).reshape(query_count, query_heads * head_size)


def finish(maxima, totals, numerator):
    head_size = numerator.shape[1] // totals.shape[1]
    return numerator / jnp.repeat(totals, head_size, axis=1)


def reference(ctx_queries, context_key_rows, context_value_rows, resp_queries, resp_keys, response_value_rows, split_index, out_weight):
    context_block_count = CONTEXT_TOKENS // CONTEXT_BLOCK
    query_blocks = ctx_queries.reshape(context_block_count, CONTEXT_BLOCK, QUERY_HEADS * HEAD_WIDTH)
    blocked_keys = context_key_rows.reshape(context_block_count, CONTEXT_BLOCK, KEY_VALUE_HEADS * HEAD_WIDTH)
    blocked_values = context_value_rows.reshape(context_block_count, CONTEXT_BLOCK, KEY_VALUE_HEADS * HEAD_WIDTH)
    anchor_keys = context_key_rows[:CONTEXT_BLOCK]
    anchor_values = context_value_rows[:CONTEXT_BLOCK]
    positions = jnp.arange(CONTEXT_BLOCK, dtype=jnp.int32)
    own_visible = positions[None, :] <= positions[:, None]

    def one_block(inputs):
        query_block, key_block, value_block, block_index = inputs
        anchor_visible = jnp.broadcast_to(block_index > 0, (CONTEXT_BLOCK, CONTEXT_BLOCK))
        visible = jnp.concatenate([anchor_visible, own_visible], axis=1)
        joined_keys = jnp.concatenate([anchor_keys, key_block], axis=0)
        joined_values = jnp.concatenate([anchor_values, value_block], axis=0)
        return finish(*partial_softmax(query_block, joined_keys, joined_values, visible, HEAD_WIDTH))

    ctx_out = lax.map(one_block, (query_blocks, blocked_keys, blocked_values, jnp.arange(context_block_count, dtype=jnp.int32)))
    ctx_out = ctx_out.reshape(CONTEXT_TOKENS, QUERY_HEADS * HEAD_WIDTH)
    response_rows = jnp.arange(RESPONSE_ROWS, dtype=jnp.int32)
    boundary = split_index[0]
    reply_visible = (response_rows[None, :] <= response_rows[:, None]) & ((response_rows[None, :] < boundary) == (response_rows[:, None] < boundary))
    visible = jnp.concatenate([jnp.ones((RESPONSE_ROWS, CONTEXT_TOKENS), dtype=bool), reply_visible], axis=1)
    all_keys = jnp.concatenate([context_key_rows, resp_keys], axis=0)
    all_values = jnp.concatenate([context_value_rows, response_value_rows], axis=0)
    attended = finish(*partial_softmax(resp_queries, all_keys, all_values, visible, HEAD_WIDTH)).astype(jnp.bfloat16)
    resp_out = jnp.dot(attended, out_weight, preferred_element_type=jnp.float32)
    return ctx_out, resp_out
```

```python
import functools

import jax
import jax.numpy as jnp
from jax import lax
from jax.experimental import pallas as pl
from jax.experimental.pallas import tpu as pltpu
from jax.sharding import PartitionSpec as P

HEAD_WIDTH = 128
NEGATIVE = -1e30
SCALE = HEAD_WIDTH ** (-0.5)
INTERPRET = False


def _dot_t(a, b):
    return lax.dot_general(a, b, (((1,), (1,)), ((), ())), preferred_element_type=jnp.float32)


def _ctx_kernel(flag_ref, q_ref, ka_ref, va_ref, ko_ref, vo_ref, o_ref):
    tq = q_ref.shape[0]
    block = ko_ref.shape[0]
    i = pl.program_id(1)
    q = q_ref[...]
    anchor_on = flag_ref[0] > 0
    s_a = _dot_t(q, ka_ref[...]) * SCALE
    s_o = _dot_t(q, ko_ref[...]) * SCALE
    rows = i * tq + lax.broadcasted_iota(jnp.int32, (tq, block), 0)
    cols = lax.broadcasted_iota(jnp.int32, (tq, block), 1)
    own_vis = cols <= rows
    s_a = jnp.where(anchor_on, s_a, NEGATIVE)
    s_o = jnp.where(own_vis, s_o, NEGATIVE)
    m = jnp.maximum(jnp.max(s_a, axis=1, keepdims=True), jnp.max(s_o, axis=1, keepdims=True))
    w_a = jnp.where(anchor_on, jnp.exp(s_a - m), 0.0)
    w_o = jnp.where(own_vis, jnp.exp(s_o - m), 0.0)
    total = jnp.sum(w_a, axis=1, keepdims=True) + jnp.sum(w_o, axis=1, keepdims=True)
    num = jnp.dot(w_a.astype(jnp.bfloat16), va_ref[...], preferred_element_type=jnp.float32)
    num = num + jnp.dot(w_o.astype(jnp.bfloat16), vo_ref[...], preferred_element_type=jnp.float32)
    o_ref[...] = num / total


def ctx_attention(flag, q, ka, va, ko, vo, tq=256):
    rows, width = q.shape
    heads = width // HEAD_WIDTH
    block = ko.shape[0]
    kv_spec = pl.BlockSpec((block, HEAD_WIDTH), lambda h, i, f: (0, 0))
    grid_spec = pltpu.PrefetchScalarGridSpec(
        num_scalar_prefetch=1,
        grid=(heads, rows // tq),
        in_specs=[
            pl.BlockSpec((tq, HEAD_WIDTH), lambda h, i, f: (i, h)),
            kv_spec, kv_spec, kv_spec, kv_spec,
        ],
        out_specs=pl.BlockSpec((tq, HEAD_WIDTH), lambda h, i, f: (i, h)),
    )
    return pl.pallas_call(
        _ctx_kernel,
        grid_spec=grid_spec,
        out_shape=jax.ShapeDtypeStruct((rows, width), jnp.float32),
        interpret=INTERPRET,
    )(flag, q, ka, va, ko, vo)


def _part_kernel(q_ref, k_ref, v_ref, num_ref, m_ref, l_ref):
    heads = q_ref.shape[1] // HEAD_WIDTH
    k = k_ref[...]
    v = v_ref[...]
    for j in range(heads):
        cols = slice(j * HEAD_WIDTH, (j + 1) * HEAD_WIDTH)
        s = _dot_t(q_ref[:, cols], k) * SCALE
        m = jnp.max(s, axis=1, keepdims=True)
        w = jnp.exp(s - m)
        m_ref[:, j:j + 1] = m
        l_ref[:, j:j + 1] = jnp.sum(w, axis=1, keepdims=True)
        num_ref[:, cols] = jnp.dot(w.astype(jnp.bfloat16), v, preferred_element_type=jnp.float32)


def part_attention(q, k, v, tq=128):
    rows = q.shape[0]
    width = q.shape[1]
    heads = width // HEAD_WIDTH
    block = k.shape[0]
    kv_spec = pl.BlockSpec((block, HEAD_WIDTH), lambda i: (0, 0))
    stat_spec = pl.BlockSpec((tq, heads), lambda i: (i, 0))
    return pl.pallas_call(
        _part_kernel,
        grid=(rows // tq,),
        in_specs=[pl.BlockSpec((tq, width), lambda i: (i, 0)), kv_spec, kv_spec],
        out_specs=[pl.BlockSpec((tq, width), lambda i: (i, 0)), stat_spec, stat_spec],
        out_shape=[
            jax.ShapeDtypeStruct((rows, width), jnp.float32),
            jax.ShapeDtypeStruct((rows, heads), jnp.float32),
            jax.ShapeDtypeStruct((rows, heads), jnp.float32),
        ],
        interpret=INTERPRET,
    )(q, k, v)


def on_device(
    ctx_queries,
    context_key_rows,
    context_value_rows,
    resp_queries,
    resp_keys,
    response_value_rows,
    split_index,
    out_weight,
):
    device = lax.axis_index("ctx")
    n_ctx = lax.axis_size("ctx")
    width = resp_queries.shape[1]
    heads = width // HEAD_WIDTH
    resp_dev = resp_queries.shape[0]

    packed = jnp.concatenate([resp_queries, resp_keys, response_value_rows], axis=1)
    gathered = lax.all_gather(packed, "ctx", axis=0, tiled=True)
    all_q = gathered[:, :width]
    all_k = gathered[:, width:width + HEAD_WIDTH]
    all_v = gathered[:, width + HEAD_WIDTH:]

    num, mx, tot = part_attention(all_q, context_key_rows, context_value_rows)
    state = jnp.concatenate([mx, tot, num], axis=1)
    state = lax.all_to_all(state, "ctx", 0, 0, tiled=True)
    state = state.reshape(n_ctx, resp_dev, -1)
    m_s = state[:, :, :heads]
    l_s = state[:, :, heads:2 * heads]
    num_s = state[:, :, 2 * heads:].reshape(n_ctx, resp_dev, heads, HEAD_WIDTH)

    own_rows = device * resp_dev + jnp.arange(resp_dev, dtype=jnp.int32)
    key_pos = jnp.arange(all_k.shape[0], dtype=jnp.int32)
    boundary = split_index[0]
    seen = (key_pos[None, :] <= own_rows[:, None]) & (
        (key_pos[None, :] < boundary) == (own_rows[:, None] < boundary)
    )
    q_own = resp_queries.reshape(resp_dev, heads, HEAD_WIDTH)
    s_r = jnp.einsum("rhd,kd->rhk", q_own, all_k, preferred_element_type=jnp.float32) * SCALE
    s_r = jnp.where(seen[:, None, :], s_r, NEGATIVE)
    m_r = jnp.max(s_r, axis=2)
    w_r = jnp.where(seen[:, None, :], jnp.exp(s_r - m_r[:, :, None]), 0.0)
    l_r = jnp.sum(w_r, axis=2)
    num_r = jnp.einsum(
        "rhk,kd->rhd", w_r.astype(jnp.bfloat16), all_v, preferred_element_type=jnp.float32
    )

    top = jnp.maximum(jnp.max(m_s, axis=0), m_r)
    f_s = jnp.exp(m_s - top[None])
    f_r = jnp.exp(m_r - top)
    total = jnp.sum(l_s * f_s, axis=0) + l_r * f_r
    numer = jnp.sum(num_s * f_s[..., None], axis=0) + num_r * f_r[..., None]
    attended = (numer / total[..., None]).reshape(resp_dev, width).astype(jnp.bfloat16)
    projected = jnp.dot(attended, out_weight, preferred_element_type=jnp.float32)
    resp_out = lax.psum_scatter(projected, "tp", scatter_dimension=1, tiled=True)

    anchor = jnp.stack([context_key_rows, context_value_rows])
    anchor = jnp.where(device == 0, anchor, jnp.zeros_like(anchor))
    anchor = lax.psum(anchor, "ctx")
    flag = (device > 0).astype(jnp.int32).reshape(1)
    ctx_out = ctx_attention(
        flag, ctx_queries, anchor[0], anchor[1], context_key_rows, context_value_rows
    )
    return (ctx_out, resp_out)


def solution(mesh):
    placed = (
        P("ctx", "tp"),
        P("ctx", "tp"),
        P("ctx", "tp"),
        P("ctx", "tp"),
        P("ctx", "tp"),
        P("ctx", "tp"),
        P(),
        P("tp", None),
    )
    return jax.shard_map(
        on_device,
        mesh=mesh,
        in_specs=placed,
        out_specs=(P("ctx", "tp"), P("ctx", "tp")),
        check_vma=False,
    )
```

```python
import functools

import jax
import jax.numpy as jnp
from jax import lax
from jax.experimental import pallas as pl
from jax.experimental.pallas import tpu as pltpu
from jax.sharding import PartitionSpec as P

HEAD_WIDTH = 128
NEGATIVE = -1e30
SCALE = HEAD_WIDTH ** (-0.5)
INTERPRET = False


def _dot_t(a, b):
    return lax.dot_general(a, b, (((1,), (1,)), ((), ())), preferred_element_type=jnp.float32)


def _ctx_kernel(flag_ref, q_ref, ka_ref, va_ref, ko_ref, vo_ref, o_ref):
    tq = q_ref.shape[0]
    block = ko_ref.shape[0]
    i = pl.program_id(1)
    q = q_ref[...]
    anchor_on = flag_ref[0] > 0
    s_a = _dot_t(q, ka_ref[...]) * SCALE
    s_o = _dot_t(q, ko_ref[...]) * SCALE
    rows = i * tq + lax.broadcasted_iota(jnp.int32, (tq, block), 0)
    cols = lax.broadcasted_iota(jnp.int32, (tq, block), 1)
    own_vis = cols <= rows
    s_a = jnp.where(anchor_on, s_a, NEGATIVE)
    s_o = jnp.where(own_vis, s_o, NEGATIVE)
    m = jnp.maximum(jnp.max(s_a, axis=1, keepdims=True), jnp.max(s_o, axis=1, keepdims=True))
    w_a = jnp.where(anchor_on, jnp.exp(s_a - m), 0.0)
    w_o = jnp.where(own_vis, jnp.exp(s_o - m), 0.0)
    total = jnp.sum(w_a, axis=1, keepdims=True) + jnp.sum(w_o, axis=1, keepdims=True)
    num = jnp.dot(w_a.astype(jnp.bfloat16), va_ref[...], preferred_element_type=jnp.float32)
    num = num + jnp.dot(w_o.astype(jnp.bfloat16), vo_ref[...], preferred_element_type=jnp.float32)
    o_ref[...] = num / total


def ctx_attention(flag, q, ka, va, ko, vo, tq=256):
    rows, width = q.shape
    heads = width // HEAD_WIDTH
    block = ko.shape[0]
    kv_spec = pl.BlockSpec((block, HEAD_WIDTH), lambda h, i, f: (0, 0))
    grid_spec = pltpu.PrefetchScalarGridSpec(
        num_scalar_prefetch=1,
        grid=(heads, rows // tq),
        in_specs=[
            pl.BlockSpec((tq, HEAD_WIDTH), lambda h, i, f: (i, h)),
            kv_spec, kv_spec, kv_spec, kv_spec,
        ],
        out_specs=pl.BlockSpec((tq, HEAD_WIDTH), lambda h, i, f: (i, h)),
    )
    return pl.pallas_call(
        _ctx_kernel,
        grid_spec=grid_spec,
        out_shape=jax.ShapeDtypeStruct((rows, width), jnp.float32),
        interpret=INTERPRET,
    )(flag, q, ka, va, ko, vo)


def _part_kernel(q_ref, k_ref, v_ref, num_ref, m_ref, l_ref):
    heads = q_ref.shape[1] // HEAD_WIDTH
    k = k_ref[...]
    v = v_ref[...]
    for j in range(heads):
        cols = slice(j * HEAD_WIDTH, (j + 1) * HEAD_WIDTH)
        s = _dot_t(q_ref[:, cols], k) * SCALE
        m = jnp.max(s, axis=1, keepdims=True)
        w = jnp.exp(s - m)
        m_ref[:, j:j + 1] = m
        l_ref[:, j:j + 1] = jnp.sum(w, axis=1, keepdims=True)
        num_ref[:, cols] = jnp.dot(w.astype(jnp.bfloat16), v, preferred_element_type=jnp.float32)


def part_attention(q, k, v, tq=128):
    rows = q.shape[0]
    width = q.shape[1]
    heads = width // HEAD_WIDTH
    block = k.shape[0]
    kv_spec = pl.BlockSpec((block, HEAD_WIDTH), lambda i: (0, 0))
    stat_spec = pl.BlockSpec((tq, heads), lambda i: (i, 0))
    return pl.pallas_call(
        _part_kernel,
        grid=(rows // tq,),
        in_specs=[pl.BlockSpec((tq, width), lambda i: (i, 0)), kv_spec, kv_spec],
        out_specs=[pl.BlockSpec((tq, width), lambda i: (i, 0)), stat_spec, stat_spec],
        out_shape=[
            jax.ShapeDtypeStruct((rows, width), jnp.float32),
            jax.ShapeDtypeStruct((rows, heads), jnp.float32),
            jax.ShapeDtypeStruct((rows, heads), jnp.float32),
        ],
        interpret=INTERPRET,
    )(q, k, v)


def gather_by_all_to_all(x, axis, n):
    copies = jnp.broadcast_to(x[None], (n,) + x.shape)
    return lax.all_to_all(copies, axis, 0, 0).reshape((n * x.shape[0],) + x.shape[1:])


def broadcast_from_first(x, axis, device, n):
    stride = n // 2
    while stride >= 1:
        pairs = [(s, s + stride) for s in range(0, n, 2 * stride)]
        got = lax.ppermute(x, axis, pairs)
        x = jnp.where(device % (2 * stride) == stride, got, x)
        stride //= 2
    return x


def on_device(
    ctx_queries,
    context_key_rows,
    context_value_rows,
    resp_queries,
    resp_keys,
    response_value_rows,
    split_index,
    out_weight,
):
    device = lax.axis_index("ctx")
    n_ctx = lax.axis_size("ctx")
    width = resp_queries.shape[1]
    heads = width // HEAD_WIDTH
    resp_dev = resp_queries.shape[0]

    packed = jnp.concatenate([resp_queries, resp_keys, response_value_rows], axis=1)
    gathered = gather_by_all_to_all(packed, "ctx", n_ctx)
    all_q = gathered[:, :width]
    all_k = gathered[:, width:width + HEAD_WIDTH]
    all_v = gathered[:, width + HEAD_WIDTH:]

    num, mx, tot = part_attention(all_q, context_key_rows, context_value_rows)
    state = jnp.concatenate([mx, tot, num], axis=1)
    state = lax.all_to_all(state, "ctx", 0, 0, tiled=True)
    state = state.reshape(n_ctx, resp_dev, -1)
    m_s = state[:, :, :heads]
    l_s = state[:, :, heads:2 * heads]
    num_s = state[:, :, 2 * heads:].reshape(n_ctx, resp_dev, heads, HEAD_WIDTH)

    own_rows = device * resp_dev + jnp.arange(resp_dev, dtype=jnp.int32)
    key_pos = jnp.arange(all_k.shape[0], dtype=jnp.int32)
    boundary = split_index[0]
    seen = (key_pos[None, :] <= own_rows[:, None]) & (
        (key_pos[None, :] < boundary) == (own_rows[:, None] < boundary)
    )
    q_own = resp_queries.reshape(resp_dev, heads, HEAD_WIDTH)
    s_r = jnp.einsum("rhd,kd->rhk", q_own, all_k, preferred_element_type=jnp.float32) * SCALE
    s_r = jnp.where(seen[:, None, :], s_r, NEGATIVE)
    m_r = jnp.max(s_r, axis=2)
    w_r = jnp.where(seen[:, None, :], jnp.exp(s_r - m_r[:, :, None]), 0.0)
    l_r = jnp.sum(w_r, axis=2)
    num_r = jnp.einsum(
        "rhk,kd->rhd", w_r.astype(jnp.bfloat16), all_v, preferred_element_type=jnp.float32
    )

    top = jnp.maximum(jnp.max(m_s, axis=0), m_r)
    f_s = jnp.exp(m_s - top[None])
    f_r = jnp.exp(m_r - top)
    total = jnp.sum(l_s * f_s, axis=0) + l_r * f_r
    numer = jnp.sum(num_s * f_s[..., None], axis=0) + num_r * f_r[..., None]
    attended = (numer / total[..., None]).reshape(resp_dev, width).astype(jnp.bfloat16)
    projected = jnp.dot(attended, out_weight, preferred_element_type=jnp.float32)
    n_tp = lax.axis_size("tp")
    projected = projected.reshape(resp_dev, n_tp, -1).transpose(1, 0, 2)
    resp_out = jnp.sum(lax.all_to_all(projected, "tp", 0, 0), axis=0)

    anchor = broadcast_from_first(
        jnp.stack([context_key_rows, context_value_rows]), "ctx", device, n_ctx
    )
    flag = (device > 0).astype(jnp.int32).reshape(1)
    ctx_out = ctx_attention(
        flag, ctx_queries, anchor[0], anchor[1], context_key_rows, context_value_rows
    )
    return (ctx_out, resp_out)


def solution(mesh):
    placed = (
        P("ctx", "tp"),
        P("ctx", "tp"),
        P("ctx", "tp"),
        P("ctx", "tp"),
        P("ctx", "tp"),
        P("ctx", "tp"),
        P(),
        P("tp", None),
    )
    return jax.shard_map(
        on_device,
        mesh=mesh,
        in_specs=placed,
        out_specs=(P("ctx", "tp"), P("ctx", "tp")),
        check_vma=False,
    )
```

```python
import functools

import jax
import jax.numpy as jnp
from jax import lax
from jax.experimental import pallas as pl
from jax.experimental.pallas import tpu as pltpu
from jax.sharding import PartitionSpec as P

HEAD_WIDTH = 128
NEGATIVE = -1e30
SCALE = HEAD_WIDTH ** (-0.5)
INTERPRET = False


def _dot_t(a, b):
    return lax.dot_general(a, b, (((1,), (1,)), ((), ())), preferred_element_type=jnp.float32)


def _own_kernel(q_ref, k_ref, v_ref, st_ref):
    tq = q_ref.shape[0]
    width = q_ref.shape[1]
    heads = width // HEAD_WIDTH
    i = pl.program_id(0)
    rows = lax.broadcasted_iota(jnp.int32, (tq, tq), 0)
    cols = lax.broadcasted_iota(jnp.int32, (tq, tq), 1)
    diag_vis = cols <= rows
    start = pl.multiple_of(i * tq, tq)
    kd = k_ref[pl.ds(start, tq), :]
    vd = v_ref[pl.ds(start, tq), :]
    for j in range(heads):
        hc = slice(j * HEAD_WIDTH, (j + 1) * HEAD_WIDTH)
        q = q_ref[:, hc]
        s = jnp.where(diag_vis, _dot_t(q, kd) * SCALE, NEGATIVE)
        m = jnp.max(s, axis=1, keepdims=True)
        p = jnp.where(diag_vis, jnp.exp(s - m), 0.0)
        l = jnp.sum(p, axis=1, keepdims=True)
        acc = jnp.dot(p.astype(jnp.bfloat16), vd, preferred_element_type=jnp.float32)

        def body(t, carry, q=q):
            m, l, acc = carry
            at = pl.multiple_of(t * tq, tq)
            s = _dot_t(q, k_ref[pl.ds(at, tq), :]) * SCALE
            m_new = jnp.maximum(m, jnp.max(s, axis=1, keepdims=True))
            a = jnp.exp(m - m_new)
            p = jnp.exp(s - m_new)
            l = a * l + jnp.sum(p, axis=1, keepdims=True)
            acc = a * acc + jnp.dot(
                p.astype(jnp.bfloat16), v_ref[pl.ds(at, tq), :], preferred_element_type=jnp.float32
            )
            return m_new, l, acc

        m, l, acc = lax.fori_loop(0, i, body, (m, l, acc))
        st_ref[:, hc] = acc
        st_ref[:, width + j:width + j + 1] = m
        st_ref[:, width + heads + j:width + heads + j + 1] = l


def own_attention(q, k, v, tq=256):
    rows, width = q.shape
    heads = width // HEAD_WIDTH
    block = k.shape[0]
    kv_spec = pl.BlockSpec((block, HEAD_WIDTH), lambda i: (0, 0))
    return pl.pallas_call(
        _own_kernel,
        grid=(rows // tq,),
        in_specs=[pl.BlockSpec((tq, width), lambda i: (i, 0)), kv_spec, kv_spec],
        out_specs=pl.BlockSpec((tq, width + 2 * heads), lambda i: (i, 0)),
        out_shape=jax.ShapeDtypeStruct((rows, width + 2 * heads), jnp.float32),
        interpret=INTERPRET,
    )(q, k, v)


def _anchor_kernel(flag_ref, q_ref, ka_ref, va_ref, st_ref, o_ref):
    width = q_ref.shape[1]
    heads = width // HEAD_WIDTH
    on = flag_ref[0] > 0

    @pl.when(on)
    def _():
        ka = ka_ref[...]
        va = va_ref[...]
        for j in range(heads):
            hc = slice(j * HEAD_WIDTH, (j + 1) * HEAD_WIDTH)
            m_o = st_ref[:, width + j:width + j + 1]
            l_o = st_ref[:, width + heads + j:width + heads + j + 1]
            s = _dot_t(q_ref[:, hc], ka) * SCALE
            m = jnp.maximum(m_o, jnp.max(s, axis=1, keepdims=True))
            p = jnp.exp(s - m)
            a = jnp.exp(m_o - m)
            l = a * l_o + jnp.sum(p, axis=1, keepdims=True)
            num = a * st_ref[:, hc] + jnp.dot(
                p.astype(jnp.bfloat16), va, preferred_element_type=jnp.float32
            )
            o_ref[:, hc] = num / l

    @pl.when(jnp.logical_not(on))
    def _():
        for j in range(heads):
            hc = slice(j * HEAD_WIDTH, (j + 1) * HEAD_WIDTH)
            o_ref[:, hc] = st_ref[:, hc] / st_ref[:, width + heads + j:width + heads + j + 1]


def anchor_attention(flag, q, ka, va, st, tq=256):
    rows, width = q.shape
    block = ka.shape[0]
    kv_spec = pl.BlockSpec((block, HEAD_WIDTH), lambda i, f: (0, 0))
    grid_spec = pltpu.PrefetchScalarGridSpec(
        num_scalar_prefetch=1,
        grid=(rows // tq,),
        in_specs=[
            pl.BlockSpec((tq, width), lambda i, f: (i, 0)),
            kv_spec,
            kv_spec,
            pl.BlockSpec((tq, st.shape[1]), lambda i, f: (i, 0)),
        ],
        out_specs=pl.BlockSpec((tq, width), lambda i, f: (i, 0)),
    )
    return pl.pallas_call(
        _anchor_kernel,
        grid_spec=grid_spec,
        out_shape=jax.ShapeDtypeStruct((rows, width), jnp.float32),
        interpret=INTERPRET,
    )(flag, q, ka, va, st)


def _part_kernel(q_ref, k_ref, v_ref, st_ref):
    width = q_ref.shape[1]
    heads = width // HEAD_WIDTH
    k = k_ref[...]
    v = v_ref[...]
    for j in range(heads):
        hc = slice(j * HEAD_WIDTH, (j + 1) * HEAD_WIDTH)
        s = _dot_t(q_ref[:, hc], k) * SCALE
        m = jnp.max(s, axis=1, keepdims=True)
        w = jnp.exp(s - m)
        st_ref[:, width + j:width + j + 1] = m
        st_ref[:, width + heads + j:width + heads + j + 1] = jnp.sum(w, axis=1, keepdims=True)
        st_ref[:, hc] = jnp.dot(w.astype(jnp.bfloat16), v, preferred_element_type=jnp.float32)


def part_attention(q, k, v, tq=128):
    rows = q.shape[0]
    width = q.shape[1]
    heads = width // HEAD_WIDTH
    block = k.shape[0]
    kv_spec = pl.BlockSpec((block, HEAD_WIDTH), lambda i: (0, 0))
    return pl.pallas_call(
        _part_kernel,
        grid=(rows // tq,),
        in_specs=[pl.BlockSpec((tq, width), lambda i: (i, 0)), kv_spec, kv_spec],
        out_specs=pl.BlockSpec((tq, width + 2 * heads), lambda i: (i, 0)),
        out_shape=jax.ShapeDtypeStruct((rows, width + 2 * heads), jnp.float32),
        interpret=INTERPRET,
    )(q, k, v)


def gather_by_all_to_all(x, axis, n):
    copies = jnp.broadcast_to(x[None], (n,) + x.shape)
    return lax.all_to_all(copies, axis, 0, 0).reshape((n * x.shape[0],) + x.shape[1:])


def broadcast_from_first(x, axis, device, n):
    stride = n // 2
    while stride >= 1:
        pairs = [(s, s + stride) for s in range(0, n, 2 * stride)]
        got = lax.ppermute(x, axis, pairs)
        x = jnp.where(device % (2 * stride) == stride, got, x)
        stride //= 2
    return x


def on_device(
    ctx_queries,
    context_key_rows,
    context_value_rows,
    resp_queries,
    resp_keys,
    response_value_rows,
    split_index,
    out_weight,
):
    device = lax.axis_index("ctx")
    n_ctx = lax.axis_size("ctx")
    width = resp_queries.shape[1]
    heads = width // HEAD_WIDTH
    resp_dev = resp_queries.shape[0]

    packed = jnp.concatenate([resp_queries, resp_keys, response_value_rows], axis=1)
    gathered = gather_by_all_to_all(packed, "ctx", n_ctx)
    all_q = gathered[:, :width]
    all_k = gathered[:, width:width + HEAD_WIDTH]
    all_v = gathered[:, width + HEAD_WIDTH:]

    state = part_attention(all_q, context_key_rows, context_value_rows)
    state = lax.all_to_all(state, "ctx", 0, 0, tiled=True)
    state = state.reshape(n_ctx, resp_dev, -1)
    num_s = state[:, :, :width].reshape(n_ctx, resp_dev, heads, HEAD_WIDTH)
    m_s = state[:, :, width:width + heads]
    l_s = state[:, :, width + heads:]

    own_rows = device * resp_dev + jnp.arange(resp_dev, dtype=jnp.int32)
    key_pos = jnp.arange(all_k.shape[0], dtype=jnp.int32)
    boundary = split_index[0]
    seen = (key_pos[None, :] <= own_rows[:, None]) & (
        (key_pos[None, :] < boundary) == (own_rows[:, None] < boundary)
    )
    q_own = resp_queries.reshape(resp_dev, heads, HEAD_WIDTH)
    s_r = jnp.einsum("rhd,kd->rhk", q_own, all_k, preferred_element_type=jnp.float32) * SCALE
    s_r = jnp.where(seen[:, None, :], s_r, NEGATIVE)
    m_r = jnp.max(s_r, axis=2)
    w_r = jnp.where(seen[:, None, :], jnp.exp(s_r - m_r[:, :, None]), 0.0)
    l_r = jnp.sum(w_r, axis=2)
    num_r = jnp.einsum(
        "rhk,kd->rhd", w_r.astype(jnp.bfloat16), all_v, preferred_element_type=jnp.float32
    )

    top = jnp.maximum(jnp.max(m_s, axis=0), m_r)
    f_s = jnp.exp(m_s - top[None])
    f_r = jnp.exp(m_r - top)
    total = jnp.sum(l_s * f_s, axis=0) + l_r * f_r
    numer = jnp.sum(num_s * f_s[..., None], axis=0) + num_r * f_r[..., None]
    attended = (numer / total[..., None]).reshape(resp_dev, width).astype(jnp.bfloat16)
    projected = jnp.dot(attended, out_weight, preferred_element_type=jnp.float32)
    n_tp = lax.axis_size("tp")
    shares = lax.all_to_all(projected, "tp", 1, 0, tiled=True)
    resp_out = jnp.sum(shares.reshape(n_tp, resp_dev, -1), axis=0)

    own_state = own_attention(ctx_queries, context_key_rows, context_value_rows)
    anchor = broadcast_from_first(
        jnp.stack([context_key_rows, context_value_rows]), "ctx", device, n_ctx
    )
    flag = (device > 0).astype(jnp.int32).reshape(1)
    ctx_out = anchor_attention(flag, ctx_queries, anchor[0], anchor[1], own_state)
    return (ctx_out, resp_out)


def solution(mesh):
    placed = (
        P("ctx", "tp"),
        P("ctx", "tp"),
        P("ctx", "tp"),
        P("ctx", "tp"),
        P("ctx", "tp"),
        P("ctx", "tp"),
        P(),
        P("tp", None),
    )
    return jax.shard_map(
        on_device,
        mesh=mesh,
        in_specs=placed,
        out_specs=(P("ctx", "tp"), P("ctx", "tp")),
        check_vma=False,
    )
```

```python
import functools

import jax
import jax.numpy as jnp
from jax import lax
from jax.experimental import pallas as pl
from jax.experimental.pallas import tpu as pltpu
from jax.sharding import PartitionSpec as P

HEAD_WIDTH = 128
NEGATIVE = -1e30
SCALE = HEAD_WIDTH ** (-0.5)
INTERPRET = False


def _dot_t(a, b):
    return lax.dot_general(a, b, (((1,), (1,)), ((), ())), preferred_element_type=jnp.float32)


def _ctx_kernel(flag_ref, q_ref, ka_ref, va_ref, ko_ref, vo_ref, o_ref):
    tq = q_ref.shape[0]
    tiles = ko_ref.shape[0] // tq
    i = pl.program_id(1)
    rows = lax.broadcasted_iota(jnp.int32, (tq, tq), 0)
    cols = lax.broadcasted_iota(jnp.int32, (tq, tq), 1)
    diag_vis = cols <= rows

    def tile(c, with_anchor):
        q = q_ref[...]
        parts = []
        if with_anchor:
            parts.append((_dot_t(q, ka_ref[...]) * SCALE, va_ref[...]))
        if c > 0:
            parts.append((_dot_t(q, ko_ref[:c * tq, :]) * SCALE, vo_ref[:c * tq, :]))
        s_d = jnp.where(diag_vis, _dot_t(q, ko_ref[c * tq:(c + 1) * tq, :]) * SCALE, NEGATIVE)
        parts.append((s_d, vo_ref[c * tq:(c + 1) * tq, :]))
        m = parts[0][0].max(axis=1, keepdims=True)
        for sc, _ in parts[1:]:
            m = jnp.maximum(m, sc.max(axis=1, keepdims=True))
        total = None
        num = None
        for sc, vals in parts:
            p = jnp.exp(sc - m)
            t = jnp.sum(p, axis=1, keepdims=True)
            n = jnp.dot(p.astype(jnp.bfloat16), vals, preferred_element_type=jnp.float32)
            total = t if total is None else total + t
            num = n if num is None else num + n
        o_ref[...] = num / total

    on = flag_ref[0] > 0
    for c in range(tiles):
        @pl.when(jnp.logical_and(i == c, on))
        def _(c=c):
            tile(c, True)

        @pl.when(jnp.logical_and(i == c, jnp.logical_not(on)))
        def _(c=c):
            tile(c, False)


def ctx_attention(flag, q, ka, va, ko, vo, tq=256):
    rows, width = q.shape
    heads = width // HEAD_WIDTH
    block = ko.shape[0]
    kv_spec = pl.BlockSpec((block, HEAD_WIDTH), lambda h, i, f: (0, 0))
    grid_spec = pltpu.PrefetchScalarGridSpec(
        num_scalar_prefetch=1,
        grid=(heads, rows // tq),
        in_specs=[
            pl.BlockSpec((tq, HEAD_WIDTH), lambda h, i, f: (i, h)),
            kv_spec, kv_spec, kv_spec, kv_spec,
        ],
        out_specs=pl.BlockSpec((tq, HEAD_WIDTH), lambda h, i, f: (i, h)),
    )
    return pl.pallas_call(
        _ctx_kernel,
        grid_spec=grid_spec,
        out_shape=jax.ShapeDtypeStruct((rows, width), jnp.float32),
        interpret=INTERPRET,
    )(flag, q, ka, va, ko, vo)


def _proj_kernel(a_ref, w_ref, o_ref):
    o_ref[...] = jnp.dot(a_ref[...], w_ref[...], preferred_element_type=jnp.float32)


def projection(a, w, tn=1024):
    rows, inner = a.shape
    cols = w.shape[1]
    return pl.pallas_call(
        _proj_kernel,
        grid=(cols // tn,),
        in_specs=[
            pl.BlockSpec((rows, inner), lambda j: (0, 0)),
            pl.BlockSpec((inner, tn), lambda j: (0, j)),
        ],
        out_specs=pl.BlockSpec((rows, tn), lambda j: (0, j)),
        out_shape=jax.ShapeDtypeStruct((rows, cols), jnp.float32),
        interpret=INTERPRET,
    )(a, w)


def _part_kernel(q_ref, k_ref, v_ref, st_ref):
    width = q_ref.shape[1]
    heads = width // HEAD_WIDTH
    k = k_ref[...]
    v = v_ref[...]
    for j in range(heads):
        hc = slice(j * HEAD_WIDTH, (j + 1) * HEAD_WIDTH)
        s = _dot_t(q_ref[:, hc], k) * SCALE
        m = jnp.max(s, axis=1, keepdims=True)
        w = jnp.exp(s - m)
        st_ref[:, width + j:width + j + 1] = m
        st_ref[:, width + heads + j:width + heads + j + 1] = jnp.sum(w, axis=1, keepdims=True)
        st_ref[:, hc] = jnp.dot(w.astype(jnp.bfloat16), v, preferred_element_type=jnp.float32)


def part_attention(q, k, v, tq=128):
    rows = q.shape[0]
    width = q.shape[1]
    heads = width // HEAD_WIDTH
    block = k.shape[0]
    kv_spec = pl.BlockSpec((block, HEAD_WIDTH), lambda i: (0, 0))
    return pl.pallas_call(
        _part_kernel,
        grid=(rows // tq,),
        in_specs=[pl.BlockSpec((tq, width), lambda i: (i, 0)), kv_spec, kv_spec],
        out_specs=pl.BlockSpec((tq, width + 2 * heads), lambda i: (i, 0)),
        out_shape=jax.ShapeDtypeStruct((rows, width + 2 * heads), jnp.float32),
        interpret=INTERPRET,
    )(q, k, v)


def gather_by_all_to_all(x, axis, n):
    copies = jnp.broadcast_to(x[None], (n,) + x.shape)
    return lax.all_to_all(copies, axis, 0, 0).reshape((n * x.shape[0],) + x.shape[1:])


def broadcast_from_first(x, axis, device, n):
    stride = n // 2
    while stride >= 1:
        pairs = [(s, s + stride) for s in range(0, n, 2 * stride)]
        got = lax.ppermute(x, axis, pairs)
        x = jnp.where(device % (2 * stride) == stride, got, x)
        stride //= 2
    return x


def on_device(
    ctx_queries,
    context_key_rows,
    context_value_rows,
    resp_queries,
    resp_keys,
    response_value_rows,
    split_index,
    out_weight,
):
    device = lax.axis_index("ctx")
    n_ctx = lax.axis_size("ctx")
    width = resp_queries.shape[1]
    heads = width // HEAD_WIDTH
    resp_dev = resp_queries.shape[0]

    packed = jnp.concatenate([resp_queries, resp_keys, response_value_rows], axis=1)
    gathered = gather_by_all_to_all(packed, "ctx", n_ctx)
    all_q = gathered[:, :width]
    all_k = gathered[:, width:width + HEAD_WIDTH]
    all_v = gathered[:, width + HEAD_WIDTH:]

    state = part_attention(all_q, context_key_rows, context_value_rows)
    state = lax.all_to_all(state, "ctx", 0, 0, tiled=True)
    state = state.reshape(n_ctx, resp_dev, -1)
    num_s = state[:, :, :width].reshape(n_ctx, resp_dev, heads, HEAD_WIDTH)
    m_s = state[:, :, width:width + heads]
    l_s = state[:, :, width + heads:]

    own_rows = device * resp_dev + jnp.arange(resp_dev, dtype=jnp.int32)
    key_pos = jnp.arange(all_k.shape[0], dtype=jnp.int32)
    boundary = split_index[0]
    seen = (key_pos[None, :] <= own_rows[:, None]) & (
        (key_pos[None, :] < boundary) == (own_rows[:, None] < boundary)
    )
    q_own = resp_queries.reshape(resp_dev, heads, HEAD_WIDTH)
    s_r = jnp.einsum("rhd,kd->rhk", q_own, all_k, preferred_element_type=jnp.float32) * SCALE
    s_r = jnp.where(seen[:, None, :], s_r, NEGATIVE)
    m_r = jnp.max(s_r, axis=2)
    w_r = jnp.where(seen[:, None, :], jnp.exp(s_r - m_r[:, :, None]), 0.0)
    l_r = jnp.sum(w_r, axis=2)
    num_r = jnp.einsum(
        "rhk,kd->rhd", w_r.astype(jnp.bfloat16), all_v, preferred_element_type=jnp.float32
    )

    top = jnp.maximum(jnp.max(m_s, axis=0), m_r)
    f_s = jnp.exp(m_s - top[None])
    f_r = jnp.exp(m_r - top)
    total = jnp.sum(l_s * f_s, axis=0) + l_r * f_r
    numer = jnp.sum(num_s * f_s[..., None], axis=0) + num_r * f_r[..., None]
    attended = (numer / total[..., None]).reshape(resp_dev, width).astype(jnp.bfloat16)
    projected = projection(attended, out_weight)
    n_tp = lax.axis_size("tp")
    shares = lax.all_to_all(projected, "tp", 1, 0, tiled=True)
    resp_out = jnp.sum(shares.reshape(n_tp, resp_dev, -1), axis=0)

    anchor = broadcast_from_first(
        jnp.stack([context_key_rows, context_value_rows]), "ctx", device, n_ctx
    )
    flag = (device > 0).astype(jnp.int32).reshape(1)
    ctx_out = ctx_attention(
        flag, ctx_queries, anchor[0], anchor[1], context_key_rows, context_value_rows
    )
    return (ctx_out, resp_out)


def solution(mesh):
    placed = (
        P("ctx", "tp"),
        P("ctx", "tp"),
        P("ctx", "tp"),
        P("ctx", "tp"),
        P("ctx", "tp"),
        P("ctx", "tp"),
        P(),
        P("tp", None),
    )
    return jax.shard_map(
        on_device,
        mesh=mesh,
        in_specs=placed,
        out_specs=(P("ctx", "tp"), P("ctx", "tp")),
        check_vma=False,
    )
```

```python
import functools

import jax
import jax.numpy as jnp
from jax import lax
from jax.experimental import pallas as pl
from jax.experimental.pallas import tpu as pltpu
from jax.sharding import PartitionSpec as P

HEAD_WIDTH = 128
NEGATIVE = -1e30
SCALE = HEAD_WIDTH ** (-0.5)
INTERPRET = False


def _dot_t(a, b):
    return lax.dot_general(a, b, (((1,), (1,)), ((), ())), preferred_element_type=jnp.float32)


def _ctx_kernel(flag_ref, q_ref, ka_ref, va_ref, ko_ref, vo_ref, o_ref):
    tq = q_ref.shape[0]
    tiles = ko_ref.shape[0] // tq
    i = pl.program_id(1)
    rows = lax.broadcasted_iota(jnp.int32, (tq, tq), 0)
    cols = lax.broadcasted_iota(jnp.int32, (tq, tq), 1)
    diag_vis = cols <= rows

    def tile(c, with_anchor):
        q = q_ref[...]
        parts = []
        if with_anchor:
            parts.append((_dot_t(q, ka_ref[...]) * SCALE, va_ref[...]))
        if c > 0:
            parts.append((_dot_t(q, ko_ref[:c * tq, :]) * SCALE, vo_ref[:c * tq, :]))
        s_d = jnp.where(diag_vis, _dot_t(q, ko_ref[c * tq:(c + 1) * tq, :]) * SCALE, NEGATIVE)
        parts.append((s_d, vo_ref[c * tq:(c + 1) * tq, :]))
        m = parts[0][0].max(axis=1, keepdims=True)
        for sc, _ in parts[1:]:
            m = jnp.maximum(m, sc.max(axis=1, keepdims=True))
        total = None
        num = None
        for sc, vals in parts:
            p = jnp.exp(sc - m)
            t = jnp.sum(p, axis=1, keepdims=True)
            n = jnp.dot(p.astype(jnp.bfloat16), vals, preferred_element_type=jnp.float32)
            total = t if total is None else total + t
            num = n if num is None else num + n
        o_ref[...] = num / total

    on = flag_ref[0] > 0
    for c in range(tiles):
        @pl.when(jnp.logical_and(i == c, on))
        def _(c=c):
            tile(c, True)

        @pl.when(jnp.logical_and(i == c, jnp.logical_not(on)))
        def _(c=c):
            tile(c, False)


def ctx_attention(flag, q, ka, va, ko, vo, tq=256):
    rows, width = q.shape
    heads = width // HEAD_WIDTH
    block = ko.shape[0]
    kv_spec = pl.BlockSpec((block, HEAD_WIDTH), lambda h, i, f: (0, 0))
    grid_spec = pltpu.PrefetchScalarGridSpec(
        num_scalar_prefetch=1,
        grid=(heads, rows // tq),
        in_specs=[
            pl.BlockSpec((tq, HEAD_WIDTH), lambda h, i, f: (i, h)),
            kv_spec, kv_spec, kv_spec, kv_spec,
        ],
        out_specs=pl.BlockSpec((tq, HEAD_WIDTH), lambda h, i, f: (i, h)),
    )
    return pl.pallas_call(
        _ctx_kernel,
        grid_spec=grid_spec,
        out_shape=jax.ShapeDtypeStruct((rows, width), jnp.float32),
        interpret=INTERPRET,
    )(flag, q, ka, va, ko, vo)


def _finish_kernel(st_ref, own_ref, w_ref, o_ref, att_ref):
    width = att_ref.shape[1]
    heads = width // HEAD_WIDTH

    @pl.when(pl.program_id(0) == 0)
    def _():
        for h in range(heads):
            hc = slice(h * HEAD_WIDTH, (h + 1) * HEAD_WIDTH)
            mc = slice(width + h, width + h + 1)
            lc = slice(width + heads + h, width + heads + h + 1)
            m_s = st_ref[:, :, mc]
            m_r = own_ref[:, mc]
            top = jnp.maximum(jnp.max(m_s, axis=0), m_r)
            f_s = jnp.exp(m_s - top[None])
            f_r = jnp.exp(m_r - top)
            total = jnp.sum(st_ref[:, :, lc] * f_s, axis=0) + own_ref[:, lc] * f_r
            numer = jnp.sum(st_ref[:, :, hc] * f_s, axis=0) + own_ref[:, hc] * f_r
            att_ref[:, hc] = (numer / total).astype(att_ref.dtype)

    o_ref[...] = jnp.dot(att_ref[...], w_ref[...], preferred_element_type=jnp.float32)


def finish_projection(state, own, w, tn=1024):
    sources, rows, packed = state.shape
    inner, cols = w.shape
    return pl.pallas_call(
        _finish_kernel,
        grid=(cols // tn,),
        in_specs=[
            pl.BlockSpec((sources, rows, packed), lambda j: (0, 0, 0)),
            pl.BlockSpec((rows, packed), lambda j: (0, 0)),
            pl.BlockSpec((inner, tn), lambda j: (0, j)),
        ],
        out_specs=pl.BlockSpec((rows, tn), lambda j: (0, j)),
        out_shape=jax.ShapeDtypeStruct((rows, cols), jnp.float32),
        scratch_shapes=[pltpu.VMEM((rows, inner), jnp.bfloat16)],
        interpret=INTERPRET,
    )(state, own, w)


def _part_kernel(q_ref, k_ref, v_ref, st_ref):
    width = q_ref.shape[1]
    heads = width // HEAD_WIDTH
    k = k_ref[...]
    v = v_ref[...]
    for j in range(heads):
        hc = slice(j * HEAD_WIDTH, (j + 1) * HEAD_WIDTH)
        s = _dot_t(q_ref[:, hc], k) * SCALE
        m = jnp.max(s, axis=1, keepdims=True)
        w = jnp.exp(s - m)
        st_ref[:, width + j:width + j + 1] = m
        st_ref[:, width + heads + j:width + heads + j + 1] = jnp.sum(w, axis=1, keepdims=True)
        st_ref[:, hc] = jnp.dot(w.astype(jnp.bfloat16), v, preferred_element_type=jnp.float32)


def part_attention(q, k, v, tq=128):
    rows = q.shape[0]
    width = q.shape[1]
    heads = width // HEAD_WIDTH
    block = k.shape[0]
    kv_spec = pl.BlockSpec((block, HEAD_WIDTH), lambda i: (0, 0))
    return pl.pallas_call(
        _part_kernel,
        grid=(rows // tq,),
        in_specs=[pl.BlockSpec((tq, width), lambda i: (i, 0)), kv_spec, kv_spec],
        out_specs=pl.BlockSpec((tq, width + 2 * heads), lambda i: (i, 0)),
        out_shape=jax.ShapeDtypeStruct((rows, width + 2 * heads), jnp.float32),
        interpret=INTERPRET,
    )(q, k, v)


def gather_by_all_to_all(x, axis, n):
    copies = jnp.broadcast_to(x[None], (n,) + x.shape)
    return lax.all_to_all(copies, axis, 0, 0).reshape((n * x.shape[0],) + x.shape[1:])


def broadcast_from_first(x, axis, device, n):
    stride = n // 2
    while stride >= 1:
        pairs = [(s, s + stride) for s in range(0, n, 2 * stride)]
        got = lax.ppermute(x, axis, pairs)
        x = jnp.where(device % (2 * stride) == stride, got, x)
        stride //= 2
    return x


def on_device(
    ctx_queries,
    context_key_rows,
    context_value_rows,
    resp_queries,
    resp_keys,
    response_value_rows,
    split_index,
    out_weight,
):
    device = lax.axis_index("ctx")
    n_ctx = lax.axis_size("ctx")
    width = resp_queries.shape[1]
    heads = width // HEAD_WIDTH
    resp_dev = resp_queries.shape[0]

    packed = jnp.concatenate([resp_queries, resp_keys, response_value_rows], axis=1)
    gathered = gather_by_all_to_all(packed, "ctx", n_ctx)
    all_q = gathered[:, :width]
    all_k = gathered[:, width:width + HEAD_WIDTH]
    all_v = gathered[:, width + HEAD_WIDTH:]

    state = part_attention(all_q, context_key_rows, context_value_rows)

    anchor = broadcast_from_first(
        jnp.stack([context_key_rows, context_value_rows]), "ctx", device, n_ctx
    )
    anchor, state = lax.optimization_barrier((anchor, state))
    state = lax.all_to_all(state, "ctx", 0, 0, tiled=True)

    flag = (device > 0).astype(jnp.int32).reshape(1)
    ctx_out = ctx_attention(
        flag, ctx_queries, anchor[0], anchor[1], context_key_rows, context_value_rows
    )
    ctx_out, state = lax.optimization_barrier((ctx_out, state))
    state = state.reshape(n_ctx, resp_dev, -1)

    own_rows = device * resp_dev + jnp.arange(resp_dev, dtype=jnp.int32)
    key_pos = jnp.arange(all_k.shape[0], dtype=jnp.int32)
    boundary = split_index[0]
    seen = (key_pos[None, :] <= own_rows[:, None]) & (
        (key_pos[None, :] < boundary) == (own_rows[:, None] < boundary)
    )
    q_own = resp_queries.reshape(resp_dev, heads, HEAD_WIDTH)
    s_r = jnp.einsum("rhd,kd->rhk", q_own, all_k, preferred_element_type=jnp.float32) * SCALE
    s_r = jnp.where(seen[:, None, :], s_r, NEGATIVE)
    m_r = jnp.max(s_r, axis=2)
    w_r = jnp.where(seen[:, None, :], jnp.exp(s_r - m_r[:, :, None]), 0.0)
    l_r = jnp.sum(w_r, axis=2)
    num_r = jnp.einsum(
        "rhk,kd->rhd", w_r.astype(jnp.bfloat16), all_v, preferred_element_type=jnp.float32
    )
    own = jnp.concatenate([num_r.reshape(resp_dev, width), m_r, l_r], axis=1)
    projected = finish_projection(state, own, out_weight)
    n_tp = lax.axis_size("tp")
    shares = lax.all_to_all(projected, "tp", 1, 0, tiled=True)
    resp_out = jnp.sum(shares.reshape(n_tp, resp_dev, -1), axis=0)
    return (ctx_out, resp_out)


def solution(mesh):
    placed = (
        P("ctx", "tp"),
        P("ctx", "tp"),
        P("ctx", "tp"),
        P("ctx", "tp"),
        P("ctx", "tp"),
        P("ctx", "tp"),
        P(),
        P("tp", None),
    )
    return jax.shard_map(
        on_device,
        mesh=mesh,
        in_specs=placed,
        out_specs=(P("ctx", "tp"), P("ctx", "tp")),
        check_vma=False,
    )
```

```python
import jax
import jax.numpy as jnp
from jax import lax
from jax.experimental import pallas as pl
from jax.experimental.pallas import tpu as pltpu
from jax.sharding import PartitionSpec as P


HEAD_WIDTH = 128
NEGATIVE = -1e30
SCALE = HEAD_WIDTH ** (-0.5)
INTERPRET = False


def _dot_t(a, b):
    return lax.dot_general(a, b, (((1,), (1,)), ((), ())), preferred_element_type=jnp.float32)


def _ctx_kernel(flag_ref, q_ref, ka_ref, va_ref, ko_ref, vo_ref, o_ref):
    tq = q_ref.shape[0]
    tiles = ko_ref.shape[0] // tq
    i = pl.program_id(1)
    rows = lax.broadcasted_iota(jnp.int32, (tq, tq), 0)
    cols = lax.broadcasted_iota(jnp.int32, (tq, tq), 1)
    diag_vis = cols <= rows

    def tile(c, with_anchor):
        q = q_ref[...]
        parts = []
        if with_anchor:
            parts.append((_dot_t(q, ka_ref[...]) * SCALE, va_ref[...]))
        if c > 0:
            parts.append((_dot_t(q, ko_ref[:c * tq, :]) * SCALE, vo_ref[:c * tq, :]))
        s_d = jnp.where(diag_vis, _dot_t(q, ko_ref[c * tq:(c + 1) * tq, :]) * SCALE, NEGATIVE)
        parts.append((s_d, vo_ref[c * tq:(c + 1) * tq, :]))
        m = parts[0][0].max(axis=1, keepdims=True)
        for sc, _ in parts[1:]:
            m = jnp.maximum(m, sc.max(axis=1, keepdims=True))
        total = None
        num = None
        for sc, vals in parts:
            p = jnp.exp(sc - m)
            t = jnp.sum(p, axis=1, keepdims=True)
            n = jnp.dot(p.astype(jnp.bfloat16), vals, preferred_element_type=jnp.float32)
            total = t if total is None else total + t
            num = n if num is None else num + n
        o_ref[...] = num / total

    on = flag_ref[0] > 0
    for c in range(tiles):
        @pl.when(jnp.logical_and(i == c, on))
        def _(c=c):
            tile(c, True)

        @pl.when(jnp.logical_and(i == c, jnp.logical_not(on)))
        def _(c=c):
            tile(c, False)


def ctx_attention(flag, q, ka, va, ko, vo, head0, nheads, into=None, tq=256):
    rows, width = q.shape
    block = ko.shape[0]
    kv_spec = pl.BlockSpec((block, HEAD_WIDTH), lambda h, i, f: (0, 0))
    in_specs = [
        pl.BlockSpec((tq, HEAD_WIDTH), lambda h, i, f: (i, h + head0)),
        kv_spec, kv_spec, kv_spec, kv_spec,
    ]
    operands = [flag, q, ka, va, ko, vo]
    kernel = _ctx_kernel
    aliases = {}
    if into is not None:
        in_specs.append(pl.BlockSpec(memory_space=pl.ANY))
        operands.append(into)
        aliases = {6: 0}

        def kernel(flag_ref, q_ref, ka_ref, va_ref, ko_ref, vo_ref, into_ref, o_ref):
            _ctx_kernel(flag_ref, q_ref, ka_ref, va_ref, ko_ref, vo_ref, o_ref)

    grid_spec = pltpu.PrefetchScalarGridSpec(
        num_scalar_prefetch=1,
        grid=(nheads, rows // tq),
        in_specs=in_specs,
        out_specs=pl.BlockSpec((tq, HEAD_WIDTH), lambda h, i, f: (i, h + head0)),
    )
    return pl.pallas_call(
        kernel,
        grid_spec=grid_spec,
        out_shape=jax.ShapeDtypeStruct((rows, width), jnp.float32),
        input_output_aliases=aliases,
        interpret=INTERPRET,
    )(*operands)


def _finish_kernel(st_ref, own_ref, w_ref, o_ref, att_ref):
    width = att_ref.shape[1]
    heads = width // HEAD_WIDTH

    @pl.when(pl.program_id(0) == 0)
    def _():
        for h in range(heads):
            hc = slice(h * HEAD_WIDTH, (h + 1) * HEAD_WIDTH)
            mc = slice(width + h, width + h + 1)
            lc = slice(width + heads + h, width + heads + h + 1)
            m_s = st_ref[:, :, mc]
            m_r = own_ref[:, mc]
            top = jnp.maximum(jnp.max(m_s, axis=0), m_r)
            f_s = jnp.exp(m_s - top[None])
            f_r = jnp.exp(m_r - top)
            total = jnp.sum(st_ref[:, :, lc] * f_s, axis=0) + own_ref[:, lc] * f_r
            numer = jnp.sum(st_ref[:, :, hc] * f_s, axis=0) + own_ref[:, hc] * f_r
            att_ref[:, hc] = (numer / total).astype(att_ref.dtype)

    o_ref[...] = jnp.dot(att_ref[...], w_ref[...], preferred_element_type=jnp.float32)


def finish_projection(state, own, w, tn=1024):
    sources, rows, packed = state.shape
    inner, cols = w.shape
    return pl.pallas_call(
        _finish_kernel,
        grid=(cols // tn,),
        in_specs=[
            pl.BlockSpec((sources, rows, packed), lambda j: (0, 0, 0)),
            pl.BlockSpec((rows, packed), lambda j: (0, 0)),
            pl.BlockSpec((inner, tn), lambda j: (0, j)),
        ],
        out_specs=pl.BlockSpec((rows, tn), lambda j: (0, j)),
        out_shape=jax.ShapeDtypeStruct((rows, cols), jnp.float32),
        scratch_shapes=[pltpu.VMEM((rows, inner), jnp.bfloat16)],
        interpret=INTERPRET,
    )(state, own, w)


def _part_kernel(q_ref, k_ref, v_ref, st_ref):
    width = q_ref.shape[1]
    heads = width // HEAD_WIDTH
    k = k_ref[...]
    v = v_ref[...]
    for j in range(heads):
        hc = slice(j * HEAD_WIDTH, (j + 1) * HEAD_WIDTH)
        s = _dot_t(q_ref[:, hc], k) * SCALE
        m = jnp.max(s, axis=1, keepdims=True)
        w = jnp.exp(s - m)
        st_ref[:, width + j:width + j + 1] = m
        st_ref[:, width + heads + j:width + heads + j + 1] = jnp.sum(w, axis=1, keepdims=True)
        st_ref[:, hc] = jnp.dot(w.astype(jnp.bfloat16), v, preferred_element_type=jnp.float32)


def part_attention(q, k, v, tq=128):
    rows = q.shape[0]
    width = q.shape[1]
    heads = width // HEAD_WIDTH
    block = k.shape[0]
    kv_spec = pl.BlockSpec((block, HEAD_WIDTH), lambda i: (0, 0))
    return pl.pallas_call(
        _part_kernel,
        grid=(rows // tq,),
        in_specs=[pl.BlockSpec((tq, width), lambda i: (i, 0)), kv_spec, kv_spec],
        out_specs=pl.BlockSpec((tq, width + 2 * heads), lambda i: (i, 0)),
        out_shape=jax.ShapeDtypeStruct((rows, width + 2 * heads), jnp.float32),
        interpret=INTERPRET,
    )(q, k, v)


def gather_by_all_to_all(x, axis, n):
    copies = jnp.broadcast_to(x[None], (n,) + x.shape)
    return lax.all_to_all(copies, axis, 0, 0).reshape((n * x.shape[0],) + x.shape[1:])


def broadcast_from_first(x, axis, device, n):
    stride = n // 2
    while stride >= 1:
        pairs = [(s, s + stride) for s in range(0, n, 2 * stride)]
        got = lax.ppermute(x, axis, pairs)
        x = jnp.where(device % (2 * stride) == stride, got, x)
        stride //= 2
    return x


def layer(
    ctx_queries,
    context_key_rows,
    context_value_rows,
    resp_queries,
    resp_keys,
    response_value_rows,
    split_index,
    out_weight,
):
    device = lax.axis_index("ctx")
    n_ctx = lax.axis_size("ctx")
    width = resp_queries.shape[1]
    heads = width // HEAD_WIDTH
    resp_dev = resp_queries.shape[0]

    packed = jnp.concatenate([resp_queries, resp_keys, response_value_rows], axis=1)
    gathered = gather_by_all_to_all(packed, "ctx", n_ctx)
    all_q = gathered[:, :width]
    all_k = gathered[:, width:width + HEAD_WIDTH]
    all_v = gathered[:, width + HEAD_WIDTH:]

    state = part_attention(all_q, context_key_rows, context_value_rows)

    anchor = broadcast_from_first(
        jnp.stack([context_key_rows, context_value_rows]), "ctx", device, n_ctx
    )
    anchor, state = lax.optimization_barrier((anchor, state))
    state = lax.all_to_all(state, "ctx", 0, 0, tiled=True)

    flag = (device > 0).astype(jnp.int32).reshape(1)
    kv = (anchor[0], anchor[1], context_key_rows, context_value_rows)
    half = (heads * 5) // 8
    ctx_out = ctx_attention(flag, ctx_queries, *kv, 0, half)
    ctx_out, state = lax.optimization_barrier((ctx_out, state))
    state = state.reshape(n_ctx, resp_dev, -1)

    own_rows = device * resp_dev + jnp.arange(resp_dev, dtype=jnp.int32)
    key_pos = jnp.arange(all_k.shape[0], dtype=jnp.int32)
    boundary = split_index[0]
    seen = (key_pos[None, :] <= own_rows[:, None]) & (
        (key_pos[None, :] < boundary) == (own_rows[:, None] < boundary)
    )
    q_own = resp_queries.reshape(resp_dev, heads, HEAD_WIDTH)
    s_r = jnp.einsum("rhd,kd->rhk", q_own, all_k, preferred_element_type=jnp.float32) * SCALE
    s_r = jnp.where(seen[:, None, :], s_r, NEGATIVE)
    m_r = jnp.max(s_r, axis=2)
    w_r = jnp.where(seen[:, None, :], jnp.exp(s_r - m_r[:, :, None]), 0.0)
    l_r = jnp.sum(w_r, axis=2)
    num_r = jnp.einsum(
        "rhk,kd->rhd", w_r.astype(jnp.bfloat16), all_v, preferred_element_type=jnp.float32
    )
    own = jnp.concatenate([num_r.reshape(resp_dev, width), m_r, l_r], axis=1)
    projected = finish_projection(state, own, out_weight)
    n_tp = lax.axis_size("tp")
    shares = lax.all_to_all(projected, "tp", 1, 0, tiled=True)
    ctx_out = ctx_attention(flag, ctx_queries, *kv, half, heads - half, into=ctx_out)
    ctx_out, shares = lax.optimization_barrier((ctx_out, shares))
    resp_out = jnp.sum(shares.reshape(n_tp, resp_dev, -1), axis=0)
    return (ctx_out, resp_out)


def solution(mesh):
    placed = (
        P("ctx", "tp"),
        P("ctx", "tp"),
        P("ctx", "tp"),
        P("ctx", "tp"),
        P("ctx", "tp"),
        P("ctx", "tp"),
        P(),
        P("tp", None),
    )
    return jax.shard_map(
        layer,
        mesh=mesh,
        in_specs=placed,
        out_specs=(P("ctx", "tp"), P("ctx", "tp")),
        check_vma=False,
    )
```

```python
import jax
import jax.numpy as jnp
from jax import lax
from jax.experimental import pallas as pl
from jax.experimental.pallas import tpu as pltpu
from jax.sharding import PartitionSpec as P


HEAD_WIDTH = 128
NEGATIVE = -1e30
SCALE = HEAD_WIDTH ** (-0.5)
INTERPRET = False


def _dot_t(a, b):
    return lax.dot_general(a, b, (((1,), (1,)), ((), ())), preferred_element_type=jnp.float32)


def _ctx_kernel(flag_ref, q_ref, ka_ref, va_ref, ko_ref, vo_ref, o_ref):
    tq = q_ref.shape[0]
    tiles = ko_ref.shape[0] // tq
    i = pl.program_id(1)
    rows = lax.broadcasted_iota(jnp.int32, (tq, tq), 0)
    cols = lax.broadcasted_iota(jnp.int32, (tq, tq), 1)
    diag_vis = cols <= rows

    def tile(c, with_anchor):
        q = q_ref[...]
        parts = []
        if with_anchor:
            parts.append((_dot_t(q, ka_ref[...]) * SCALE, va_ref[...]))
        if c > 0:
            parts.append((_dot_t(q, ko_ref[:c * tq, :]) * SCALE, vo_ref[:c * tq, :]))
        s_d = jnp.where(diag_vis, _dot_t(q, ko_ref[c * tq:(c + 1) * tq, :]) * SCALE, NEGATIVE)
        parts.append((s_d, vo_ref[c * tq:(c + 1) * tq, :]))
        m = parts[0][0].max(axis=1, keepdims=True)
        for sc, _ in parts[1:]:
            m = jnp.maximum(m, sc.max(axis=1, keepdims=True))
        total = None
        num = None
        for sc, vals in parts:
            p = jnp.exp(sc - m)
            t = jnp.sum(p, axis=1, keepdims=True)
            n = jnp.dot(p.astype(jnp.bfloat16), vals, preferred_element_type=jnp.float32)
            total = t if total is None else total + t
            num = n if num is None else num + n
        o_ref[...] = num / total

    on = flag_ref[0] > 0
    for c in range(tiles):
        @pl.when(jnp.logical_and(i == c, on))
        def _(c=c):
            tile(c, True)

        @pl.when(jnp.logical_and(i == c, jnp.logical_not(on)))
        def _(c=c):
            tile(c, False)


def ctx_attention(flag, q, ka, va, ko, vo, head0, nheads, into=None, tq=256):
    rows, width = q.shape
    block = ko.shape[0]
    kv_spec = pl.BlockSpec((block, HEAD_WIDTH), lambda h, i, f: (0, 0))
    in_specs = [
        pl.BlockSpec((tq, HEAD_WIDTH), lambda h, i, f: (i, h + head0)),
        kv_spec, kv_spec, kv_spec, kv_spec,
    ]
    operands = [flag, q, ka, va, ko, vo]
    kernel = _ctx_kernel
    aliases = {}
    if into is not None:
        in_specs.append(pl.BlockSpec(memory_space=pl.ANY))
        operands.append(into)
        aliases = {6: 0}

        def kernel(flag_ref, q_ref, ka_ref, va_ref, ko_ref, vo_ref, into_ref, o_ref):
            _ctx_kernel(flag_ref, q_ref, ka_ref, va_ref, ko_ref, vo_ref, o_ref)

    grid_spec = pltpu.PrefetchScalarGridSpec(
        num_scalar_prefetch=1,
        grid=(nheads, rows // tq),
        in_specs=in_specs,
        out_specs=pl.BlockSpec((tq, HEAD_WIDTH), lambda h, i, f: (i, h + head0)),
    )
    return pl.pallas_call(
        kernel,
        grid_spec=grid_spec,
        out_shape=jax.ShapeDtypeStruct((rows, width), jnp.float32),
        input_output_aliases=aliases,
        interpret=INTERPRET,
    )(*operands)


def _finish_kernel(st_ref, own_ref, w_ref, o_ref, att_ref):
    width = att_ref.shape[1]
    heads = width // HEAD_WIDTH

    @pl.when(pl.program_id(0) == 0)
    def _():
        for h in range(heads):
            hc = slice(h * HEAD_WIDTH, (h + 1) * HEAD_WIDTH)
            mc = slice(width + h, width + h + 1)
            lc = slice(width + heads + h, width + heads + h + 1)
            m_s = st_ref[:, :, mc]
            m_r = own_ref[:, mc]
            top = jnp.maximum(jnp.max(m_s, axis=0), m_r)
            f_s = jnp.exp(m_s - top[None])
            f_r = jnp.exp(m_r - top)
            total = jnp.sum(st_ref[:, :, lc] * f_s, axis=0) + own_ref[:, lc] * f_r
            numer = jnp.sum(st_ref[:, :, hc] * f_s, axis=0) + own_ref[:, hc] * f_r
            att_ref[:, hc] = (numer / total).astype(att_ref.dtype)

    o_ref[...] = jnp.dot(att_ref[...], w_ref[...], preferred_element_type=jnp.float32)


def finish_projection(state, own, w, tn):
    sources, rows, packed = state.shape
    inner, cols = w.shape
    return pl.pallas_call(
        _finish_kernel,
        grid=(cols // tn,),
        in_specs=[
            pl.BlockSpec((sources, rows, packed), lambda j: (0, 0, 0)),
            pl.BlockSpec((rows, packed), lambda j: (0, 0)),
            pl.BlockSpec((inner, tn), lambda j: (0, j)),
        ],
        out_specs=pl.BlockSpec((None, rows, tn), lambda j: (j, 0, 0)),
        out_shape=jax.ShapeDtypeStruct((cols // tn, rows, tn), jnp.float32),
        scratch_shapes=[pltpu.VMEM((rows, inner), jnp.bfloat16)],
        interpret=INTERPRET,
    )(state, own, w)


def _part_kernel(q_ref, k_ref, v_ref, st_ref):
    width = q_ref.shape[1]
    heads = width // HEAD_WIDTH
    k = k_ref[...]
    v = v_ref[...]
    for j in range(heads):
        hc = slice(j * HEAD_WIDTH, (j + 1) * HEAD_WIDTH)
        s = _dot_t(q_ref[:, hc], k) * SCALE
        m = jnp.max(s, axis=1, keepdims=True)
        w = jnp.exp(s - m)
        st_ref[:, width + j:width + j + 1] = m
        st_ref[:, width + heads + j:width + heads + j + 1] = jnp.sum(w, axis=1, keepdims=True)
        st_ref[:, hc] = jnp.dot(w.astype(jnp.bfloat16), v, preferred_element_type=jnp.float32)


def part_attention(q, k, v, tq=128):
    rows = q.shape[0]
    width = q.shape[1]
    heads = width // HEAD_WIDTH
    block = k.shape[0]
    kv_spec = pl.BlockSpec((block, HEAD_WIDTH), lambda i: (0, 0))
    return pl.pallas_call(
        _part_kernel,
        grid=(rows // tq,),
        in_specs=[pl.BlockSpec((tq, width), lambda i: (i, 0)), kv_spec, kv_spec],
        out_specs=pl.BlockSpec((tq, width + 2 * heads), lambda i: (i, 0)),
        out_shape=jax.ShapeDtypeStruct((rows, width + 2 * heads), jnp.float32),
        interpret=INTERPRET,
    )(q, k, v)


def gather_by_all_to_all(x, axis, n):
    copies = jnp.broadcast_to(x[None], (n,) + x.shape)
    return lax.all_to_all(copies, axis, 0, 0).reshape((n * x.shape[0],) + x.shape[1:])


def broadcast_from_first(x, axis, device, n):
    stride = n // 2
    while stride >= 1:
        pairs = [(s, s + stride) for s in range(0, n, 2 * stride)]
        got = lax.ppermute(x, axis, pairs)
        x = jnp.where(device % (2 * stride) == stride, got, x)
        stride //= 2
    return x


def layer(
    ctx_queries,
    context_key_rows,
    context_value_rows,
    resp_queries,
    resp_keys,
    response_value_rows,
    split_index,
    out_weight,
):
    device = lax.axis_index("ctx")
    n_ctx = lax.axis_size("ctx")
    width = resp_queries.shape[1]
    heads = width // HEAD_WIDTH
    resp_dev = resp_queries.shape[0]

    packed = jnp.concatenate([resp_queries, resp_keys, response_value_rows], axis=1)
    gathered = gather_by_all_to_all(packed, "ctx", n_ctx)
    all_q = gathered[:, :width]
    all_k = gathered[:, width:width + HEAD_WIDTH]
    all_v = gathered[:, width + HEAD_WIDTH:]

    state = part_attention(all_q, context_key_rows, context_value_rows)

    anchor = broadcast_from_first(
        jnp.stack([context_key_rows, context_value_rows]), "ctx", device, n_ctx
    )
    state = lax.all_to_all(state, "ctx", 0, 0, tiled=True)

    flag = (device > 0).astype(jnp.int32).reshape(1)
    kv = (anchor[0], anchor[1], context_key_rows, context_value_rows)
    half = (heads * 5) // 8
    ctx_out = ctx_attention(flag, ctx_queries, *kv, 0, half)
    ctx_out, state = lax.optimization_barrier((ctx_out, state))
    state = state.reshape(n_ctx, resp_dev, -1)

    own_rows = device * resp_dev + jnp.arange(resp_dev, dtype=jnp.int32)
    key_pos = jnp.arange(all_k.shape[0], dtype=jnp.int32)
    boundary = split_index[0]
    seen = (key_pos[None, :] <= own_rows[:, None]) & (
        (key_pos[None, :] < boundary) == (own_rows[:, None] < boundary)
    )
    q_own = resp_queries.reshape(resp_dev, heads, HEAD_WIDTH)
    s_r = jnp.einsum("rhd,kd->rhk", q_own, all_k, preferred_element_type=jnp.float32) * SCALE
    s_r = jnp.where(seen[:, None, :], s_r, NEGATIVE)
    m_r = jnp.max(s_r, axis=2)
    w_r = jnp.where(seen[:, None, :], jnp.exp(s_r - m_r[:, :, None]), 0.0)
    l_r = jnp.sum(w_r, axis=2)
    num_r = jnp.einsum(
        "rhk,kd->rhd", w_r.astype(jnp.bfloat16), all_v, preferred_element_type=jnp.float32
    )
    own = jnp.concatenate([num_r.reshape(resp_dev, width), m_r, l_r], axis=1)
    n_tp = lax.axis_size("tp")
    projected = finish_projection(state, own, out_weight, out_weight.shape[1] // n_tp)
    shares = lax.all_to_all(projected, "tp", 0, 0, tiled=True)
    ctx_out = ctx_attention(flag, ctx_queries, *kv, half, heads - half, into=ctx_out)
    ctx_out, shares = lax.optimization_barrier((ctx_out, shares))
    resp_out = jnp.sum(shares.reshape(n_tp, resp_dev, -1), axis=0)
    return (ctx_out, resp_out)


def solution(mesh):
    placed = (
        P("ctx", "tp"),
        P("ctx", "tp"),
        P("ctx", "tp"),
        P("ctx", "tp"),
        P("ctx", "tp"),
        P("ctx", "tp"),
        P(),
        P("tp", None),
    )
    return jax.shard_map(
        layer,
        mesh=mesh,
        in_specs=placed,
        out_specs=(P("ctx", "tp"), P("ctx", "tp")),
        check_vma=False,
    )
```

```python
import jax
import jax.numpy as jnp
from jax import lax
from jax.experimental import pallas as pl
from jax.experimental.pallas import tpu as pltpu
from jax.sharding import PartitionSpec as P


HEAD_WIDTH = 128
NEGATIVE = -1e30
SCALE = HEAD_WIDTH ** (-0.5)
INTERPRET = False


def _dot_t(a, b):
    return lax.dot_general(a, b, (((1,), (1,)), ((), ())), preferred_element_type=jnp.float32)


def _ctx_kernel(flag_ref, q_ref, ka_ref, va_ref, ko_ref, vo_ref, o_ref):
    tq = q_ref.shape[0]
    tiles = ko_ref.shape[0] // tq
    i = pl.program_id(1)
    rows = lax.broadcasted_iota(jnp.int32, (tq, tq), 0)
    cols = lax.broadcasted_iota(jnp.int32, (tq, tq), 1)
    diag_vis = cols <= rows

    def tile(c, with_anchor):
        q = q_ref[...]
        parts = []
        if with_anchor:
            parts.append((_dot_t(q, ka_ref[...]) * SCALE, va_ref[...]))
        if c > 0:
            parts.append((_dot_t(q, ko_ref[:c * tq, :]) * SCALE, vo_ref[:c * tq, :]))
        s_d = jnp.where(diag_vis, _dot_t(q, ko_ref[c * tq:(c + 1) * tq, :]) * SCALE, NEGATIVE)
        parts.append((s_d, vo_ref[c * tq:(c + 1) * tq, :]))
        m = parts[0][0].max(axis=1, keepdims=True)
        for sc, _ in parts[1:]:
            m = jnp.maximum(m, sc.max(axis=1, keepdims=True))
        total = None
        num = None
        for sc, vals in parts:
            p = jnp.exp(sc - m)
            t = jnp.sum(p, axis=1, keepdims=True)
            n = jnp.dot(p.astype(jnp.bfloat16), vals, preferred_element_type=jnp.float32)
            total = t if total is None else total + t
            num = n if num is None else num + n
        o_ref[...] = num / total

    on = flag_ref[0] > 0
    for c in range(tiles):
        @pl.when(jnp.logical_and(i == c, on))
        def _(c=c):
            tile(c, True)

        @pl.when(jnp.logical_and(i == c, jnp.logical_not(on)))
        def _(c=c):
            tile(c, False)


def ctx_attention(flag, q, anchor, ko, vo, head0, nheads, into=None, tq=256):
    rows, width = q.shape
    block = ko.shape[0]
    kv_spec = pl.BlockSpec((block, HEAD_WIDTH), lambda h, i, f: (0, 0))
    in_specs = [
        pl.BlockSpec((tq, HEAD_WIDTH), lambda h, i, f: (i, h + head0)),
        pl.BlockSpec((None, block, HEAD_WIDTH), lambda h, i, f: (0, 0, 0)),
        pl.BlockSpec((None, block, HEAD_WIDTH), lambda h, i, f: (1, 0, 0)),
        kv_spec, kv_spec,
    ]
    operands = [flag, q, anchor, anchor, ko, vo]
    kernel = _ctx_kernel
    aliases = {}
    if into is not None:
        in_specs.append(pl.BlockSpec(memory_space=pl.ANY))
        operands.append(into)
        aliases = {6: 0}

        def kernel(flag_ref, q_ref, ka_ref, va_ref, ko_ref, vo_ref, into_ref, o_ref):
            _ctx_kernel(flag_ref, q_ref, ka_ref, va_ref, ko_ref, vo_ref, o_ref)

    grid_spec = pltpu.PrefetchScalarGridSpec(
        num_scalar_prefetch=1,
        grid=(nheads, rows // tq),
        in_specs=in_specs,
        out_specs=pl.BlockSpec((tq, HEAD_WIDTH), lambda h, i, f: (i, h + head0)),
    )
    return pl.pallas_call(
        kernel,
        grid_spec=grid_spec,
        out_shape=jax.ShapeDtypeStruct((rows, width), jnp.float32),
        input_output_aliases=aliases,
        interpret=INTERPRET,
    )(*operands)


def _finish_kernel(st_ref, own_ref, w_ref, o_ref, att_ref):
    width = att_ref.shape[1]
    heads = width // HEAD_WIDTH

    @pl.when(pl.program_id(0) == 0)
    def _():
        for h in range(heads):
            hc = slice(h * HEAD_WIDTH, (h + 1) * HEAD_WIDTH)
            mc = slice(width + h, width + h + 1)
            lc = slice(width + heads + h, width + heads + h + 1)
            m_s = st_ref[:, :, mc]
            m_r = own_ref[:, mc]
            top = jnp.maximum(jnp.max(m_s, axis=0), m_r)
            f_s = jnp.exp(m_s - top[None])
            f_r = jnp.exp(m_r - top)
            total = jnp.sum(st_ref[:, :, lc] * f_s, axis=0) + own_ref[:, lc] * f_r
            numer = jnp.sum(st_ref[:, :, hc] * f_s, axis=0) + own_ref[:, hc] * f_r
            att_ref[:, hc] = (numer / total).astype(att_ref.dtype)

    o_ref[...] = jnp.dot(att_ref[...], w_ref[...], preferred_element_type=jnp.float32)


def finish_projection(state, own, w, tn):
    sources, rows, packed = state.shape
    inner, cols = w.shape
    return pl.pallas_call(
        _finish_kernel,
        grid=(cols // tn,),
        in_specs=[
            pl.BlockSpec((sources, rows, packed), lambda j: (0, 0, 0)),
            pl.BlockSpec((rows, packed), lambda j: (0, 0)),
            pl.BlockSpec((inner, tn), lambda j: (0, j)),
        ],
        out_specs=pl.BlockSpec((None, rows, tn), lambda j: (j, 0, 0)),
        out_shape=jax.ShapeDtypeStruct((cols // tn, rows, tn), jnp.float32),
        scratch_shapes=[pltpu.VMEM((rows, inner), jnp.bfloat16)],
        interpret=INTERPRET,
    )(state, own, w)


def _part_kernel(q_ref, k_ref, v_ref, st_ref):
    width = q_ref.shape[1]
    heads = width // HEAD_WIDTH
    k = k_ref[...]
    v = v_ref[...]
    for j in range(heads):
        hc = slice(j * HEAD_WIDTH, (j + 1) * HEAD_WIDTH)
        s = _dot_t(q_ref[:, hc], k) * SCALE
        m = jnp.max(s, axis=1, keepdims=True)
        w = jnp.exp(s - m)
        st_ref[:, width + j:width + j + 1] = m
        st_ref[:, width + heads + j:width + heads + j + 1] = jnp.sum(w, axis=1, keepdims=True)
        st_ref[:, hc] = jnp.dot(w.astype(jnp.bfloat16), v, preferred_element_type=jnp.float32)


def part_attention(q, k, v, tq=128):
    rows = q.shape[0]
    width = q.shape[1]
    heads = width // HEAD_WIDTH
    block = k.shape[0]
    kv_spec = pl.BlockSpec((block, HEAD_WIDTH), lambda i: (0, 0))
    return pl.pallas_call(
        _part_kernel,
        grid=(rows // tq,),
        in_specs=[pl.BlockSpec((tq, width), lambda i: (i, 0)), kv_spec, kv_spec],
        out_specs=pl.BlockSpec((tq, width + 2 * heads), lambda i: (i, 0)),
        out_shape=jax.ShapeDtypeStruct((rows, width + 2 * heads), jnp.float32),
        interpret=INTERPRET,
    )(q, k, v)


def gather_by_all_to_all(x, axis, n):
    copies = jnp.broadcast_to(x[None], (n,) + x.shape)
    return lax.all_to_all(copies, axis, 0, 0).reshape((n * x.shape[0],) + x.shape[1:])


def broadcast_from_first(x, axis, device, n):
    stride = n // 2
    while stride >= 1:
        pairs = [(s, s + stride) for s in range(0, n, 2 * stride)]
        got = lax.ppermute(x, axis, pairs)
        x = jnp.where(device % (2 * stride) == stride, got, x)
        stride //= 2
    return x


def layer(
    ctx_queries,
    context_key_rows,
    context_value_rows,
    resp_queries,
    resp_keys,
    response_value_rows,
    split_index,
    out_weight,
):
    device = lax.axis_index("ctx")
    n_ctx = lax.axis_size("ctx")
    width = resp_queries.shape[1]
    heads = width // HEAD_WIDTH
    resp_dev = resp_queries.shape[0]

    packed = jnp.concatenate([resp_queries, resp_keys, response_value_rows], axis=1)
    gathered = gather_by_all_to_all(packed, "ctx", n_ctx)
    all_q = gathered[:, :width]
    all_k = gathered[:, width:width + HEAD_WIDTH]
    all_v = gathered[:, width + HEAD_WIDTH:]

    state = part_attention(all_q, context_key_rows, context_value_rows)

    anchor = broadcast_from_first(
        jnp.stack([context_key_rows, context_value_rows]), "ctx", device, n_ctx
    )
    state = lax.all_to_all(state, "ctx", 0, 0, tiled=True)

    flag = (device > 0).astype(jnp.int32).reshape(1)
    kv = (anchor, context_key_rows, context_value_rows)
    half = (heads * 5) // 8
    ctx_out = ctx_attention(flag, ctx_queries, *kv, 0, half)
    ctx_out, state = lax.optimization_barrier((ctx_out, state))
    state = state.reshape(n_ctx, resp_dev, -1)

    own_rows = device * resp_dev + jnp.arange(resp_dev, dtype=jnp.int32)
    key_pos = jnp.arange(all_k.shape[0], dtype=jnp.int32)
    boundary = split_index[0]
    seen = (key_pos[None, :] <= own_rows[:, None]) & (
        (key_pos[None, :] < boundary) == (own_rows[:, None] < boundary)
    )
    q_own = resp_queries.reshape(resp_dev, heads, HEAD_WIDTH)
    s_r = jnp.einsum("rhd,kd->rhk", q_own, all_k, preferred_element_type=jnp.float32) * SCALE
    s_r = jnp.where(seen[:, None, :], s_r, NEGATIVE)
    m_r = jnp.max(s_r, axis=2)
    w_r = jnp.where(seen[:, None, :], jnp.exp(s_r - m_r[:, :, None]), 0.0)
    l_r = jnp.sum(w_r, axis=2)
    num_r = jnp.einsum(
        "rhk,kd->rhd", w_r.astype(jnp.bfloat16), all_v, preferred_element_type=jnp.float32
    )
    own = jnp.concatenate([num_r.reshape(resp_dev, width), m_r, l_r], axis=1)
    n_tp = lax.axis_size("tp")
    projected = finish_projection(state, own, out_weight, out_weight.shape[1] // n_tp)
    shares = lax.all_to_all(projected, "tp", 0, 0, tiled=True)
    ctx_out = ctx_attention(flag, ctx_queries, *kv, half, heads - half, into=ctx_out)
    ctx_out, shares = lax.optimization_barrier((ctx_out, shares))
    resp_out = jnp.sum(shares.reshape(n_tp, resp_dev, -1), axis=0)
    return (ctx_out, resp_out)


def solution(mesh):
    placed = (
        P("ctx", "tp"),
        P("ctx", "tp"),
        P("ctx", "tp"),
        P("ctx", "tp"),
        P("ctx", "tp"),
        P("ctx", "tp"),
        P(),
        P("tp", None),
    )
    return jax.shard_map(
        layer,
        mesh=mesh,
        in_specs=placed,
        out_specs=(P("ctx", "tp"), P("ctx", "tp")),
        check_vma=False,
    )
```
